256 devices in a mesh: row: 16 (over x, y), col: 16 (over z, core).
Axes of the slice: x: 4, y: 4, z: 8, core: 2. Of those that a mesh axis runs over, the one named last changes fastest.
Arguments:
- rhs: float32 [4, 16, 16, 128, 256], P(None, 'row', 'col'), may hold values from -6 to 6
- diag_inverse: float32 [4, 16, 16, 128, 128], P(None, 'row', 'col'), as said below
- update_blocks: float32 [3, 16, 16, 48, 128, 128], P(None, 'row', 'col'), may hold values from -0.15625 to 0.15625
- source_slot: int32 [3, 16, 16, 48], P(None, 'row', 'col'), may hold values from 0 to 15
- target_slot: int32 [3, 16, 16, 48], P(None, 'row', 'col'), may hold values from 0 to 15
- block_count: int32 [3, 16, 16], P(None, 'row', 'col'), may hold values from 1 to 48, as said below
Outputs:
- forward_solution: float32 [4, 16, 16, 128, 256], P(None, 'row', 'col')
- solution: float32 [4, 16, 16, 128, 256], P(None, 'row', 'col')
The draws below stay inside these ranges and needn't reach their ends.
Inputs may be any that keep to these rules, and one draw needn't show every extreme that they name: Each diag_inverse block is lower triangular with diagonal entries between 0.5 and 1.6. `block_count`: at every level some device uses all 48 slots.
All inputs are finite; a program needn't handle non-finite values.
Results may differ from the reference program's by a relative error of at most 0.0003.
Values sent between devices are 32-bit elements; how exact they have to be, the bound alone decides.
No kernel may reach another device: no remote copies, remote signals or barrier semaphores. Data moves between devices by JAX's collectives and lax.ppermute only.
A program may use at most 128 MiB of HBM per device.

```python
import math
import jax
import jax.numpy as jnp
from jax import lax

S = 128
NRHS = 256
LEVELS = 4
NB = 48
ROWS_SN = 16
COLS_SN = 16


def draw_diag_inverse(key, part):
    key_diag, second = jax.random.split(key)
    layout = (LEVELS, ROWS_SN, COLS_SN, S)
    diagonal = jnp.exp(jax.random.uniform(key_diag, layout, jnp.float32, math.log(0.5), math.log(1.6)))
    lower_part = jnp.clip(jax.random.normal(second, layout + (S,), jnp.float32), -4.0, 4.0) * (0.6 / math.sqrt(S))
    row_index = jnp.arange(S)[:, None]
    col_index = jnp.arange(S)[None, :]
    strict = jnp.where(row_index > col_index, lower_part, 0.0)
    return strict + jnp.where(row_index == col_index, 1.0, 0.0) * diagonal[..., :, None]


def draw_block_count(key, part):
    key_first, key_second, key_full = jax.random.split(key, 3)
    layout = (LEVELS - 1, ROWS_SN * COLS_SN)
    multiplier = jax.random.randint(key_first, layout, 1, NB + 1)
    multiplicand = jax.random.randint(key_second, layout, 1, NB + 1)
    filled = (multiplier * multiplicand + NB - 1) // NB
    busiest = jax.random.randint(key_full, (LEVELS - 1, 1), 0, ROWS_SN * COLS_SN)
    filled = jnp.where(jnp.arange(ROWS_SN * COLS_SN)[None, :] == busiest, NB, filled)
    return filled.reshape(LEVELS - 1, ROWS_SN, COLS_SN).astype(jnp.int32)


def place_ends(array, key, smallest, largest):
    longest = array.shape.index(max(array.shape))
    spots = []
    for shift in (0, 1):
        where = [jax.random.randint(jax.random.fold_in(key, axis), (), 0, length) for axis, length in enumerate(array.shape)]
        where[longest] = (where[longest] + shift) % array.shape[longest]
        spots.append(tuple(where))
    return array.at[spots[0]].set(smallest).at[spots[1]].set(largest)


def shard_levels(key, shape, cuts, low, top_value):
    def one(axis_at, blocks):
        heights = jax.random.uniform(jax.random.fold_in(jax.random.fold_in(key, 6), axis_at), (blocks,), jnp.float32, low / len(cuts), top_value / len(cuts))
        return jnp.repeat(jnp.exp(heights), shape[axis_at] // blocks).reshape((-1,) + (1,) * (len(shape) - axis_at - 1))

    gain = one(*cuts[0])
    for cut in cuts[1:]:
        gain = gain * one(*cut)
    return gain


def noise(key, shape, spread, reach, shards=(), kind=jnp.bfloat16):
    drawn = spread * jax.random.normal(key, shape, jnp.float32)
    if shards:
        drawn = drawn * shard_levels(key, shape, shards, -0.22, 0.18)
    return jnp.clip(drawn, -reach, reach).astype(kind)


def setup_inputs(seed: int = 0) -> dict:
    streams_of = jax.random.split(jax.random.key(seed), 7)
    return {
        "rhs": noise(streams_of[0], (LEVELS, ROWS_SN, COLS_SN, S, NRHS), 1.0, 6.0, ((1, 16), (2, 16)), jnp.float32),
        "diag_inverse": draw_diag_inverse(jax.random.fold_in(streams_of[6], 71), 0),
        "update_blocks": noise(streams_of[2], (LEVELS - 1, ROWS_SN, COLS_SN, NB, S, S), (S * NB // 4) ** -0.5, 0.15625, ((1, 16), (2, 16)), jnp.float32),
        "source_slot": place_ends(jax.random.randint(streams_of[3], (LEVELS - 1, ROWS_SN, COLS_SN, NB), 0, ROWS_SN), jax.random.fold_in(streams_of[3], 1), 0, ROWS_SN - 1).astype(jnp.int32),
        "target_slot": place_ends(jax.random.randint(streams_of[4], (LEVELS - 1, ROWS_SN, COLS_SN, NB), 0, COLS_SN), jax.random.fold_in(streams_of[4], 1), 0, COLS_SN - 1).astype(jnp.int32),
        "block_count": draw_block_count(jax.random.fold_in(streams_of[6], 71), 0),
    }


def apply_inverse(inverse, values):
    return jnp.einsum("...st,...tn->...sn", inverse, values, precision=lax.Precision.HIGHEST)


def apply_transposed(inverse, values):
    return jnp.einsum("...ts,...tn->...sn", inverse, values, precision=lax.Precision.HIGHEST)


def reference(rhs, diag_inverse, update_blocks, source_slot, target_slot, block_count):
    precise = lax.Precision.HIGHEST
    levels, row_count, col_count, block_width, right_count = rhs.shape
    slot_count = update_blocks.shape[3]
    columns = jnp.arange(col_count, dtype=jnp.int32)[:, None]
    forward = [apply_inverse(diag_inverse[0], rhs[0])]
    for level_index in range(1, levels):
        previous = forward[-1]

        def row_terms(inputs, previous=previous):
            tile_stack, sources, targets, filled = inputs
            active = (jnp.arange(slot_count, dtype=jnp.int32)[None, :] < filled[:, None]).astype(jnp.float32)
            chosen = previous[sources, columns]
            products = jnp.einsum("cbst,cbtn->cbsn", tile_stack, chosen, precision=precise) * active[:, :, None, None]
            base_terms = jnp.zeros((col_count, block_width, right_count), jnp.float32)
            return base_terms.at[targets.reshape(-1)].add(products.reshape(-1, block_width, right_count))

        updates = lax.map(row_terms, (update_blocks[level_index - 1], source_slot[level_index - 1],
                                      target_slot[level_index - 1], block_count[level_index - 1]))
        forward.append(apply_inverse(diag_inverse[level_index], rhs[level_index] - updates))
    backward = [apply_transposed(diag_inverse[levels - 1], forward[levels - 1])]
    for level_index in range(levels - 2, -1, -1):
        following = backward[0]

        def row_back(totals, inputs):
            tile_stack, sources, targets, filled, solved_row = inputs
            active = (jnp.arange(slot_count, dtype=jnp.int32)[None, :] < filled[:, None]).astype(jnp.float32)
            chosen = solved_row[targets]
            products = jnp.einsum("cbts,cbtn->cbsn", tile_stack, chosen, precision=precise) * active[:, :, None, None]
            return totals.at[sources, columns].add(products), None

        start_totals = jnp.zeros((row_count, col_count, block_width, right_count), jnp.float32)
        totals, unused = lax.scan(row_back, start_totals,
                                  (update_blocks[level_index], source_slot[level_index], target_slot[level_index],
                                   block_count[level_index], following))
        backward.insert(0, apply_transposed(diag_inverse[level_index], forward[level_index] - totals))
    return jnp.stack(forward), jnp.stack(backward)
```

```python
import functools
import math

import jax
import jax.numpy as jnp
from jax import lax
from jax.experimental import pallas as pl
from jax.experimental.pallas import tpu as pltpu
from jax.sharding import PartitionSpec as P

GROUP = 8


def apply_inverse(inverse, values):
    return jnp.einsum("...st,...tn->...sn", inverse, values, precision=lax.Precision.HIGHEST)


def apply_transposed(inverse, values):
    return jnp.einsum("...ts,...tn->...sn", inverse, values, precision=lax.Precision.HIGHEST)


def _terms_kernel(transposed, group, picked_ref, placed_ref, filled_ref, tiles_ref, operand_ref, out_ref):
    step = pl.program_id(0)

    @pl.when(step == 0)
    def _():
        out_ref[...] = jnp.zeros_like(out_ref)

    filled = filled_ref[0]
    for g in range(group):
        b = step * group + g

        @pl.when(b < filled)
        def _():
            source = picked_ref[b]
            target = placed_ref[b]
            tile = tiles_ref[g]
            values = operand_ref[source]
            if transposed:
                product = lax.dot_general(tile, values, (((0,), (0,)), ((), ())),
                                          precision=lax.Precision.HIGHEST, preferred_element_type=jnp.float32)
            else:
                product = jnp.dot(tile, values, precision=lax.Precision.HIGHEST, preferred_element_type=jnp.float32)
            out_ref[target] += product


def block_terms_kernel(tile_stack, picked, placed, filled, operand, count, transposed):
    slot_count, s, _ = tile_stack.shape
    n_src, _, width = operand.shape
    group = math.gcd(slot_count, GROUP)
    steps = slot_count // group

    def tile_map(j, picked_ref, placed_ref, filled_ref):
        last = jnp.maximum(filled_ref[0] - 1, 0) // group
        return (jnp.minimum(j, last), 0, 0)

    grid_spec = pltpu.PrefetchScalarGridSpec(
        num_scalar_prefetch=3,
        grid=(steps,),
        in_specs=[
            pl.BlockSpec((group, s, s), tile_map),
            pl.BlockSpec((n_src, s, width), lambda j, *_: (0, 0, 0)),
        ],
        out_specs=pl.BlockSpec((count, s, width), lambda j, *_: (0, 0, 0)),
    )
    flops = 2 * slot_count * s * s * width
    return pl.pallas_call(
        functools.partial(_terms_kernel, transposed, group),
        grid_spec=grid_spec,
        out_shape=jax.ShapeDtypeStruct((count, s, width), jnp.float32),
        compiler_params=pltpu.CompilerParams(dimension_semantics=("arbitrary",)),
        cost_estimate=pl.CostEstimate(flops=flops, bytes_accessed=4 * (slot_count * s * s + 2 * n_src * s * width), transcendentals=0),
    )(jnp.clip(picked, 0, n_src - 1), jnp.clip(placed, 0, count - 1), jnp.reshape(filled, (1,)), tile_stack, operand)


def block_terms(tile_stack, picked, placed, filled, operand, totals, transposed):
    return block_terms_kernel(tile_stack, picked, placed, filled, operand, totals.shape[0], transposed)


def gather_blocks(block, axis, count):
    stacked = jnp.broadcast_to(block[None], (count,) + block.shape)
    return lax.all_to_all(stacked, axis, 0, 0, tiled=True)


def scatter_sum(parts, axis):
    return lax.all_to_all(parts, axis, 0, 0, tiled=True).sum(axis=0)


def per_device(rhs, diag_inverse, update_blocks, source_slot, target_slot, block_count):
    levels = rhs.shape[0]
    last_level = levels - 1
    rhs_local = rhs[:, 0, 0]
    inverse_local = diag_inverse[:, 0, 0]
    tiles_local = update_blocks[:, 0, 0]
    sources_local = source_slot[:, 0, 0]
    targets_local = target_slot[:, 0, 0]
    filled_local = block_count[:, 0, 0]
    row_count = lax.axis_size("row")
    col_count = lax.axis_size("col")
    block_shape = rhs_local.shape[1:]
    forward = [apply_inverse(inverse_local[0], rhs_local[0])]
    for level_index in range(1, levels):
        forward_gathered = gather_blocks(forward[-1], "row", row_count)
        forward_zero_terms = jnp.zeros((col_count,) + block_shape, jnp.float32)
        owner_reduced = scatter_sum(
            block_terms(
                tiles_local[level_index - 1],
                sources_local[level_index - 1],
                targets_local[level_index - 1],
                filled_local[level_index - 1],
                forward_gathered,
                forward_zero_terms,
                False,
            ),
            "col",
        )
        forward.append(
            apply_inverse(inverse_local[level_index], rhs_local[level_index] - owner_reduced)
        )
    backward = [apply_transposed(inverse_local[last_level], forward[-1])]
    for level_index in range(last_level - 1, -1, -1):
        gathered = gather_blocks(backward[0], "col", col_count)
        solved = forward[level_index]
        zero_terms = jnp.zeros((row_count,) + block_shape, jnp.float32)
        totals = block_terms(
            tiles_local[level_index],
            targets_local[level_index],
            sources_local[level_index],
            filled_local[level_index],
            gathered,
            zero_terms,
            True,
        )
        reduced = scatter_sum(totals, "row")
        backward.insert(0, apply_transposed(inverse_local[level_index], solved - reduced))
    forward_out = jnp.stack(forward)[:, None, None]
    backward_out = jnp.stack(backward)[:, None, None]
    return (forward_out, backward_out)


def solution(mesh):
    in_specs = (
        P(None, "row", "col", None, None),
        P(None, "row", "col", None, None),
        P(None, "row", "col", None, None, None),
        P(None, "row", "col", None),
        P(None, "row", "col", None),
        P(None, "row", "col"),
    )
    out_specs = (P(None, "row", "col", None, None), P(None, "row", "col", None, None))
    return jax.shard_map(
        per_device, mesh=mesh, in_specs=in_specs, out_specs=out_specs, check_vma=False
    )
```

```python
import functools
import math

import jax
import jax.numpy as jnp
from jax import lax
from jax.experimental import pallas as pl
from jax.experimental.pallas import tpu as pltpu
from jax.sharding import Mesh
from jax.sharding import PartitionSpec as P

GROUP = 8


def apply_inverse(inverse, values):
    return jnp.einsum("...st,...tn->...sn", inverse, values, precision=lax.Precision.HIGHEST)


def apply_transposed(inverse, values):
    return jnp.einsum("...ts,...tn->...sn", inverse, values, precision=lax.Precision.HIGHEST)


def _terms_kernel(transposed, group, picked_ref, placed_ref, filled_ref, tiles_ref, operand_ref, out_ref):
    step = pl.program_id(0)

    @pl.when(step == 0)
    def _():
        out_ref[...] = jnp.zeros_like(out_ref)

    filled = filled_ref[0]
    for g in range(group):
        b = step * group + g

        @pl.when(b < filled)
        def _():
            source = picked_ref[b]
            target = placed_ref[b]
            tile = tiles_ref[g]
            values = operand_ref[source]
            if transposed:
                product = lax.dot_general(tile, values, (((0,), (0,)), ((), ())),
                                          precision=lax.Precision.HIGHEST, preferred_element_type=jnp.float32)
            else:
                product = jnp.dot(tile, values, precision=lax.Precision.HIGHEST, preferred_element_type=jnp.float32)
            out_ref[target] += product


def block_terms_kernel(tile_stack, picked, placed, filled, operand, count, transposed):
    slot_count, s, _ = tile_stack.shape
    n_src, _, width = operand.shape
    group = math.gcd(slot_count, GROUP)
    steps = slot_count // group

    def tile_map(j, picked_ref, placed_ref, filled_ref):
        last = jnp.maximum(filled_ref[0] - 1, 0) // group
        return (jnp.minimum(j, last), 0, 0)

    grid_spec = pltpu.PrefetchScalarGridSpec(
        num_scalar_prefetch=3,
        grid=(steps,),
        in_specs=[
            pl.BlockSpec((group, s, s), tile_map),
            pl.BlockSpec((n_src, s, width), lambda j, *_: (0, 0, 0)),
        ],
        out_specs=pl.BlockSpec((count, s, width), lambda j, *_: (0, 0, 0)),
    )
    flops = 2 * slot_count * s * s * width
    return pl.pallas_call(
        functools.partial(_terms_kernel, transposed, group),
        grid_spec=grid_spec,
        out_shape=jax.ShapeDtypeStruct((count, s, width), jnp.float32),
        compiler_params=pltpu.CompilerParams(dimension_semantics=("arbitrary",)),
        cost_estimate=pl.CostEstimate(flops=flops, bytes_accessed=4 * (slot_count * s * s + 2 * n_src * s * width), transcendentals=0),
    )(jnp.clip(picked, 0, n_src - 1), jnp.clip(placed, 0, count - 1), jnp.reshape(filled, (1,)), tile_stack, operand)


def block_terms(tile_stack, picked, placed, filled, operand, totals, transposed):
    return block_terms_kernel(tile_stack, picked, placed, filled, operand, totals.shape[0], transposed)


def gather_blocks(block, axis, count):
    stacked = jnp.broadcast_to(block[None], (count,) + block.shape)
    return lax.all_to_all(stacked, axis, 0, 0, tiled=True)


def scatter_sum(parts, axis):
    return lax.all_to_all(parts, axis, 0, 0, tiled=True).sum(axis=0)


def column_slot(position):
    cores = lax.axis_size("core")
    return (position % cores) * lax.axis_size("chip") + position // cores


def gather_columns(block):
    chips = lax.axis_size("chip")
    cores = lax.axis_size("core")
    by_chip = gather_blocks(block, "chip", chips)
    stacked = jnp.broadcast_to(by_chip[None], (cores,) + by_chip.shape)
    both = lax.all_to_all(stacked, "core", 0, 0, tiled=True)
    return both.reshape((cores * chips,) + block.shape)


def scatter_columns(parts):
    chips = lax.axis_size("chip")
    cores = lax.axis_size("core")
    by_core = parts.reshape((cores, chips) + parts.shape[1:])
    chip_sums = lax.all_to_all(by_core, "core", 0, 0, tiled=True).sum(axis=0)
    return scatter_sum(chip_sums, "chip")


def per_device(rhs, diag_inverse, update_blocks, source_slot, target_slot, block_count):
    levels = rhs.shape[0]
    last_level = levels - 1
    rhs_local = rhs[:, 0, 0]
    inverse_local = diag_inverse[:, 0, 0]
    tiles_local = update_blocks[:, 0, 0]
    sources_local = source_slot[:, 0, 0]
    targets_local = target_slot[:, 0, 0]
    filled_local = block_count[:, 0, 0]
    row_count = lax.axis_size("row")
    col_count = lax.axis_size("chip") * lax.axis_size("core")
    block_shape = rhs_local.shape[1:]
    forward = [apply_inverse(inverse_local[0], rhs_local[0])]
    for level_index in range(1, levels):
        forward_gathered = gather_blocks(forward[-1], "row", row_count)
        forward_zero_terms = jnp.zeros((col_count,) + block_shape, jnp.float32)
        owner_reduced = scatter_columns(
            block_terms(
                tiles_local[level_index - 1],
                sources_local[level_index - 1],
                column_slot(targets_local[level_index - 1]),
                filled_local[level_index - 1],
                forward_gathered,
                forward_zero_terms,
                False,
            ),
        )
        forward.append(
            apply_inverse(inverse_local[level_index], rhs_local[level_index] - owner_reduced)
        )
    backward = [apply_transposed(inverse_local[last_level], forward[-1])]
    for level_index in range(last_level - 1, -1, -1):
        gathered = gather_columns(backward[0])
        solved = forward[level_index]
        zero_terms = jnp.zeros((row_count,) + block_shape, jnp.float32)
        totals = block_terms(
            tiles_local[level_index],
            column_slot(targets_local[level_index]),
            sources_local[level_index],
            filled_local[level_index],
            gathered,
            zero_terms,
            True,
        )
        reduced = scatter_sum(totals, "row")
        backward.insert(0, apply_transposed(inverse_local[level_index], solved - reduced))
    forward_out = jnp.stack(forward)[:, None, None]
    backward_out = jnp.stack(backward)[:, None, None]
    return (forward_out, backward_out)


def solution(mesh):
    rows, cols = mesh.devices.shape
    split = Mesh(mesh.devices.reshape(rows, cols // 2, 2), ("row", "chip", "core"))
    col = ("chip", "core")
    in_specs = (
        P(None, "row", col, None, None),
        P(None, "row", col, None, None),
        P(None, "row", col, None, None, None),
        P(None, "row", col, None),
        P(None, "row", col, None),
        P(None, "row", col),
    )
    out_specs = (P(None, "row", col, None, None), P(None, "row", col, None, None))
    return jax.shard_map(
        per_device, mesh=split, in_specs=in_specs, out_specs=out_specs, check_vma=False
    )
```

```python
import functools
import math

import jax
import jax.numpy as jnp
from jax import lax
from jax.experimental import pallas as pl
from jax.experimental.pallas import tpu as pltpu
from jax.sharding import Mesh
from jax.sharding import PartitionSpec as P

GROUP = 8
CHUNKS = 2


def apply_inverse(inverse, values):
    return jnp.einsum("...st,...tn->...sn", inverse, values, precision=lax.Precision.HIGHEST)


def apply_transposed(inverse, values):
    return jnp.einsum("...ts,...tn->...sn", inverse, values, precision=lax.Precision.HIGHEST)


def _terms_kernel(transposed, group, picked_ref, placed_ref, filled_ref, tiles_ref, operand_ref, out_ref):
    step = pl.program_id(0)

    @pl.when(step == 0)
    def _():
        out_ref[...] = jnp.zeros_like(out_ref)

    filled = filled_ref[0]
    for g in range(group):
        b = step * group + g

        @pl.when(b < filled)
        def _():
            source = picked_ref[b]
            target = placed_ref[b]
            tile = tiles_ref[g]
            values = operand_ref[source]
            if transposed:
                product = lax.dot_general(tile, values, (((0,), (0,)), ((), ())),
                                          precision=lax.Precision.HIGHEST, preferred_element_type=jnp.float32)
            else:
                product = jnp.dot(tile, values, precision=lax.Precision.HIGHEST, preferred_element_type=jnp.float32)
            out_ref[target] += product


def block_terms_kernel(tile_stack, picked, placed, filled, operand, count, transposed):
    slot_count, s, _ = tile_stack.shape
    n_src, _, width = operand.shape
    group = math.gcd(slot_count, GROUP)
    steps = slot_count // group

    def tile_map(j, picked_ref, placed_ref, filled_ref):
        last = jnp.maximum(filled_ref[0] - 1, 0) // group
        return (jnp.minimum(j, last), 0, 0)

    grid_spec = pltpu.PrefetchScalarGridSpec(
        num_scalar_prefetch=3,
        grid=(steps,),
        in_specs=[
            pl.BlockSpec((group, s, s), tile_map),
            pl.BlockSpec((n_src, s, width), lambda j, *_: (0, 0, 0)),
        ],
        out_specs=pl.BlockSpec((count, s, width), lambda j, *_: (0, 0, 0)),
    )
    flops = 2 * slot_count * s * s * width
    return pl.pallas_call(
        functools.partial(_terms_kernel, transposed, group),
        grid_spec=grid_spec,
        out_shape=jax.ShapeDtypeStruct((count, s, width), jnp.float32),
        compiler_params=pltpu.CompilerParams(dimension_semantics=("arbitrary",)),
        cost_estimate=pl.CostEstimate(flops=flops, bytes_accessed=4 * (slot_count * s * s + 2 * n_src * s * width), transcendentals=0),
    )(jnp.clip(picked, 0, n_src - 1), jnp.clip(placed, 0, count - 1), jnp.reshape(filled, (1,)), tile_stack, operand)


def block_terms(tile_stack, picked, placed, filled, operand, totals, transposed):
    return block_terms_kernel(tile_stack, picked, placed, filled, operand, totals.shape[0], transposed)


def gather_blocks(block, axis, count):
    stacked = jnp.broadcast_to(block[None], (count,) + block.shape)
    return lax.all_to_all(stacked, axis, 0, 0, tiled=True)


def scatter_sum(parts, axis):
    return lax.all_to_all(parts, axis, 0, 0, tiled=True).sum(axis=0)


def shifted(value, axis, count, shift):
    return lax.ppermute(value, axis, [(j, (j + shift) % count) for j in range(count)])


def gather_slot(position):
    cores = lax.axis_size("core")
    chips = lax.axis_size("chip")
    core_rel = (position % cores - lax.axis_index("core")) % cores
    chip_rel = (lax.axis_index("chip") - position // cores) % chips
    return core_rel * chips + chip_rel


def scatter_slot(position):
    cores = lax.axis_size("core")
    chips = lax.axis_size("chip")
    core_rel = (position % cores - lax.axis_index("core")) % cores
    chip_rel = (position // cores - lax.axis_index("chip")) % chips
    return core_rel * chips + chip_rel


def gather_columns(block):
    chips = lax.axis_size("chip")
    by_chip = jnp.stack([block] + [shifted(block, "chip", chips, k) for k in range(1, chips)])
    other = shifted(by_chip, "core", lax.axis_size("core"), 1)
    return jnp.concatenate([by_chip, other], axis=0)


def scatter_columns(parts):
    chips = lax.axis_size("chip")
    mine = parts[:chips] + shifted(parts[chips:], "core", lax.axis_size("core"), 1)
    total = mine[0]
    for k in range(1, chips):
        total = total + shifted(mine[k], "chip", chips, k)
    return total


def solve_columns(rhs_local, inverse_local, tiles_local, sources_local, targets_local, filled_local):
    levels = rhs_local.shape[0]
    last_level = levels - 1
    row_count = lax.axis_size("row")
    col_count = lax.axis_size("chip") * lax.axis_size("core")
    block_shape = rhs_local.shape[1:]
    forward = [apply_inverse(inverse_local[0], rhs_local[0])]
    for level_index in range(1, levels):
        forward_gathered = gather_blocks(forward[-1], "row", row_count)
        forward_zero_terms = jnp.zeros((col_count,) + block_shape, jnp.float32)
        owner_reduced = scatter_columns(
            block_terms(
                tiles_local[level_index - 1],
                sources_local[level_index - 1],
                scatter_slot(targets_local[level_index - 1]),
                filled_local[level_index - 1],
                forward_gathered,
                forward_zero_terms,
                False,
            ),
        )
        forward.append(
            apply_inverse(inverse_local[level_index], rhs_local[level_index] - owner_reduced)
        )
    backward = [apply_transposed(inverse_local[last_level], forward[-1])]
    for level_index in range(last_level - 1, -1, -1):
        gathered = gather_columns(backward[0])
        solved = forward[level_index]
        zero_terms = jnp.zeros((row_count,) + block_shape, jnp.float32)
        totals = block_terms(
            tiles_local[level_index],
            gather_slot(targets_local[level_index]),
            sources_local[level_index],
            filled_local[level_index],
            gathered,
            zero_terms,
            True,
        )
        reduced = scatter_sum(totals, "row")
        backward.insert(0, apply_transposed(inverse_local[level_index], solved - reduced))
    return jnp.stack(forward), jnp.stack(backward)


def per_device(rhs, diag_inverse, update_blocks, source_slot, target_slot, block_count):
    rhs_local = rhs[:, 0, 0]
    shared = (diag_inverse[:, 0, 0], update_blocks[:, 0, 0], source_slot[:, 0, 0], target_slot[:, 0, 0],
              block_count[:, 0, 0])
    width = rhs_local.shape[-1]
    chunks = CHUNKS if width % (CHUNKS * 128) == 0 else 1
    step = width // chunks
    results = [solve_columns(rhs_local[..., k * step:(k + 1) * step], *shared) for k in range(chunks)]
    forward_out = jnp.concatenate([r[0] for r in results], axis=-1)[:, None, None]
    backward_out = jnp.concatenate([r[1] for r in results], axis=-1)[:, None, None]
    return (forward_out, backward_out)


def solution(mesh):
    rows, cols = mesh.devices.shape
    split = Mesh(mesh.devices.reshape(rows, cols // 2, 2), ("row", "chip", "core"))
    col = ("chip", "core")
    in_specs = (
        P(None, "row", col, None, None),
        P(None, "row", col, None, None),
        P(None, "row", col, None, None, None),
        P(None, "row", col, None),
        P(None, "row", col, None),
        P(None, "row", col),
    )
    out_specs = (P(None, "row", col, None, None), P(None, "row", col, None, None))
    return jax.shard_map(
        per_device, mesh=split, in_specs=in_specs, out_specs=out_specs, check_vma=False
    )
```

```python
import functools
import math

import jax
import jax.numpy as jnp
from jax import lax
from jax.experimental import pallas as pl
from jax.experimental.pallas import tpu as pltpu
from jax.sharding import Mesh
from jax.sharding import PartitionSpec as P

GROUP = 8


def apply_inverse(inverse, values):
    return jnp.einsum("...st,...tn->...sn", inverse, values, precision=lax.Precision.HIGHEST)


def apply_transposed(inverse, values):
    return jnp.einsum("...ts,...tn->...sn", inverse, values, precision=lax.Precision.HIGHEST)


def _split(values):
    high = values.astype(jnp.bfloat16)
    low = (values - high.astype(jnp.float32)).astype(jnp.bfloat16)
    return high, low


def _terms_kernel(transposed, group, picked_ref, placed_ref, filled_ref, tiles_ref, operand_ref, out_ref, split_ref):
    step = pl.program_id(0)

    @pl.when(step == 0)
    def _():
        out_ref[...] = jnp.zeros_like(out_ref)
        for source in range(operand_ref.shape[0]):
            high, low = _split(operand_ref[source])
            split_ref[source] = jnp.concatenate([high, low, high], axis=0)

    filled = filled_ref[0]
    for g in range(group):
        b = step * group + g

        @pl.when(b < filled)
        def _():
            high, low = _split(tiles_ref[g])
            values = split_ref[picked_ref[b]]
            if transposed:
                stacked = jnp.concatenate([high, high, low], axis=0)
                product = lax.dot_general(stacked, values, (((0,), (0,)), ((), ())),
                                          preferred_element_type=jnp.float32)
            else:
                stacked = jnp.concatenate([high, high, low], axis=1)
                product = jnp.dot(stacked, values, preferred_element_type=jnp.float32)
            out_ref[placed_ref[b]] += product


def block_terms_kernel(tile_stack, picked, placed, filled, operand, count, transposed):
    slot_count, s, _ = tile_stack.shape
    n_src, _, width = operand.shape
    group = math.gcd(slot_count, GROUP)
    steps = slot_count // group

    def tile_map(j, picked_ref, placed_ref, filled_ref):
        last = jnp.maximum(filled_ref[0] - 1, 0) // group
        return (jnp.minimum(j, last), 0, 0)

    grid_spec = pltpu.PrefetchScalarGridSpec(
        num_scalar_prefetch=3,
        grid=(steps,),
        in_specs=[
            pl.BlockSpec((group, s, s), tile_map),
            pl.BlockSpec((n_src, s, width), lambda j, *_: (0, 0, 0)),
        ],
        out_specs=pl.BlockSpec((count, s, width), lambda j, *_: (0, 0, 0)),
        scratch_shapes=[pltpu.VMEM((n_src, 3 * s, width), jnp.bfloat16)],
    )
    flops = 2 * slot_count * s * s * width
    return pl.pallas_call(
        functools.partial(_terms_kernel, transposed, group),
        grid_spec=grid_spec,
        out_shape=jax.ShapeDtypeStruct((count, s, width), jnp.float32),
        compiler_params=pltpu.CompilerParams(dimension_semantics=("arbitrary",)),
        cost_estimate=pl.CostEstimate(flops=flops, bytes_accessed=4 * (slot_count * s * s + 2 * n_src * s * width), transcendentals=0),
    )(jnp.clip(picked, 0, n_src - 1), jnp.clip(placed, 0, count - 1), jnp.reshape(filled, (1,)), tile_stack, operand)


def block_terms(tile_stack, picked, placed, filled, operand, totals, transposed):
    return block_terms_kernel(tile_stack, picked, placed, filled, operand, totals.shape[0], transposed)


def gather_blocks(block, axis, count):
    stacked = jnp.broadcast_to(block[None], (count,) + block.shape)
    return lax.all_to_all(stacked, axis, 0, 0, tiled=True)


def scatter_sum(parts, axis):
    return lax.all_to_all(parts, axis, 0, 0, tiled=True).sum(axis=0)


def column_slot(position):
    cores = lax.axis_size("core")
    return (position % cores) * lax.axis_size("chip") + position // cores


def gather_columns(block):
    chips = lax.axis_size("chip")
    cores = lax.axis_size("core")
    by_chip = gather_blocks(block, "chip", chips)
    stacked = jnp.broadcast_to(by_chip[None], (cores,) + by_chip.shape)
    both = lax.all_to_all(stacked, "core", 0, 0, tiled=True)
    return both.reshape((cores * chips,) + block.shape)


def scatter_columns(parts):
    chips = lax.axis_size("chip")
    cores = lax.axis_size("core")
    by_core = parts.reshape((cores, chips) + parts.shape[1:])
    chip_sums = lax.all_to_all(by_core, "core", 0, 0, tiled=True).sum(axis=0)
    return scatter_sum(chip_sums, "chip")


def per_device(rhs, diag_inverse, update_blocks, source_slot, target_slot, block_count):
    levels = rhs.shape[0]
    last_level = levels - 1
    rhs_local = rhs[:, 0, 0]
    inverse_local = diag_inverse[:, 0, 0]
    tiles_local = update_blocks[:, 0, 0]
    sources_local = source_slot[:, 0, 0]
    targets_local = target_slot[:, 0, 0]
    filled_local = block_count[:, 0, 0]
    row_count = lax.axis_size("row")
    col_count = lax.axis_size("chip") * lax.axis_size("core")
    block_shape = rhs_local.shape[1:]
    forward = [apply_inverse(inverse_local[0], rhs_local[0])]
    for level_index in range(1, levels):
        forward_gathered = gather_blocks(forward[-1], "row", row_count)
        forward_zero_terms = jnp.zeros((col_count,) + block_shape, jnp.float32)
        owner_reduced = scatter_columns(
            block_terms(
                tiles_local[level_index - 1],
                sources_local[level_index - 1],
                column_slot(targets_local[level_index - 1]),
                filled_local[level_index - 1],
                forward_gathered,
                forward_zero_terms,
                False,
            ),
        )
        forward.append(
            apply_inverse(inverse_local[level_index], rhs_local[level_index] - owner_reduced)
        )
    backward = [apply_transposed(inverse_local[last_level], forward[-1])]
    for level_index in range(last_level - 1, -1, -1):
        gathered = gather_columns(backward[0])
        solved = forward[level_index]
        zero_terms = jnp.zeros((row_count,) + block_shape, jnp.float32)
        totals = block_terms(
            tiles_local[level_index],
            column_slot(targets_local[level_index]),
            sources_local[level_index],
            filled_local[level_index],
            gathered,
            zero_terms,
            True,
        )
        reduced = scatter_sum(totals, "row")
        backward.insert(0, apply_transposed(inverse_local[level_index], solved - reduced))
    forward_out = jnp.stack(forward)[:, None, None]
    backward_out = jnp.stack(backward)[:, None, None]
    return (forward_out, backward_out)


def solution(mesh):
    rows, cols = mesh.devices.shape
    split = Mesh(mesh.devices.reshape(rows, cols // 2, 2), ("row", "chip", "core"))
    col = ("chip", "core")
    in_specs = (
        P(None, "row", col, None, None),
        P(None, "row", col, None, None),
        P(None, "row", col, None, None, None),
        P(None, "row", col, None),
        P(None, "row", col, None),
        P(None, "row", col),
    )
    out_specs = (P(None, "row", col, None, None), P(None, "row", col, None, None))
    return jax.shard_map(
        per_device, mesh=split, in_specs=in_specs, out_specs=out_specs, check_vma=False
    )
```

```python
import functools
import math

import jax
import jax.numpy as jnp
from jax import lax
from jax.experimental import pallas as pl
from jax.experimental.pallas import tpu as pltpu
from jax.sharding import Mesh
from jax.sharding import PartitionSpec as P

GROUP = 8
CHUNKS = 2


def apply_inverse(inverse, values):
    return jnp.einsum("...st,...tn->...sn", inverse, values, precision=lax.Precision.HIGHEST)


def apply_transposed(inverse, values):
    return jnp.einsum("...ts,...tn->...sn", inverse, values, precision=lax.Precision.HIGHEST)


def _split(values):
    high = values.astype(jnp.bfloat16)
    low = (values - high.astype(jnp.float32)).astype(jnp.bfloat16)
    return high, low


def _terms_kernel(transposed, group, picked_ref, placed_ref, filled_ref, tiles_ref, operand_ref, out_ref, split_ref):
    step = pl.program_id(0)

    @pl.when(step == 0)
    def _():
        out_ref[...] = jnp.zeros_like(out_ref)
        for source in range(operand_ref.shape[0]):
            high, low = _split(operand_ref[source])
            split_ref[source] = jnp.concatenate([high, low, high], axis=0)

    filled = filled_ref[0]

    def one_block(g, carry):
        b = step * group + g

        @pl.when(b < filled)
        def _():
            high, low = _split(tiles_ref[g])
            values = split_ref[picked_ref[b]]
            if transposed:
                stacked = jnp.concatenate([high, high, low], axis=0)
                product = lax.dot_general(stacked, values, (((0,), (0,)), ((), ())),
                                          preferred_element_type=jnp.float32)
            else:
                stacked = jnp.concatenate([high, high, low], axis=1)
                product = jnp.dot(stacked, values, preferred_element_type=jnp.float32)
            out_ref[placed_ref[b]] += product

        return carry

    lax.fori_loop(0, group, one_block, 0)


def block_terms_kernel(tile_stack, picked, placed, filled, operand, count, transposed):
    slot_count, s, _ = tile_stack.shape
    n_src, _, width = operand.shape
    group = math.gcd(slot_count, GROUP)
    steps = slot_count // group

    def tile_map(j, picked_ref, placed_ref, filled_ref):
        last = jnp.maximum(filled_ref[0] - 1, 0) // group
        return (jnp.minimum(j, last), 0, 0)

    grid_spec = pltpu.PrefetchScalarGridSpec(
        num_scalar_prefetch=3,
        grid=(steps,),
        in_specs=[
            pl.BlockSpec((group, s, s), tile_map),
            pl.BlockSpec((n_src, s, width), lambda j, *_: (0, 0, 0)),
        ],
        out_specs=pl.BlockSpec((count, s, width), lambda j, *_: (0, 0, 0)),
        scratch_shapes=[pltpu.VMEM((n_src, 3 * s, width), jnp.bfloat16)],
    )
    flops = 2 * slot_count * s * s * width
    return pl.pallas_call(
        functools.partial(_terms_kernel, transposed, group),
        grid_spec=grid_spec,
        out_shape=jax.ShapeDtypeStruct((count, s, width), jnp.float32),
        compiler_params=pltpu.CompilerParams(dimension_semantics=("arbitrary",)),
        cost_estimate=pl.CostEstimate(flops=flops, bytes_accessed=4 * (slot_count * s * s + 2 * n_src * s * width), transcendentals=0),
    )(jnp.clip(picked, 0, n_src - 1), jnp.clip(placed, 0, count - 1), jnp.reshape(filled, (1,)), tile_stack, operand)


def block_terms(tile_stack, picked, placed, filled, operand, totals, transposed):
    return block_terms_kernel(tile_stack, picked, placed, filled, operand, totals.shape[0], transposed)


def gather_blocks(block, axis, count):
    stacked = jnp.broadcast_to(block[None], (count,) + block.shape)
    return lax.all_to_all(stacked, axis, 0, 0, tiled=True)


def scatter_sum(parts, axis):
    return lax.all_to_all(parts, axis, 0, 0, tiled=True).sum(axis=0)


def column_slot(position):
    cores = lax.axis_size("core")
    return (position % cores) * lax.axis_size("chip") + position // cores


def gather_columns(block):
    chips = lax.axis_size("chip")
    cores = lax.axis_size("core")
    by_chip = gather_blocks(block, "chip", chips)
    stacked = jnp.broadcast_to(by_chip[None], (cores,) + by_chip.shape)
    both = lax.all_to_all(stacked, "core", 0, 0, tiled=True)
    return both.reshape((cores * chips,) + block.shape)


def scatter_columns(parts):
    chips = lax.axis_size("chip")
    cores = lax.axis_size("core")
    by_core = parts.reshape((cores, chips) + parts.shape[1:])
    chip_sums = lax.all_to_all(by_core, "core", 0, 0, tiled=True).sum(axis=0)
    return scatter_sum(chip_sums, "chip")


def solve_columns(rhs_local, inverse_local, tiles_local, sources_local, targets_local, filled_local):
    levels = rhs_local.shape[0]
    last_level = levels - 1
    row_count = lax.axis_size("row")
    col_count = lax.axis_size("chip") * lax.axis_size("core")
    block_shape = rhs_local.shape[1:]
    forward = [apply_inverse(inverse_local[0], rhs_local[0])]
    for level_index in range(1, levels):
        forward_gathered = gather_blocks(forward[-1], "row", row_count)
        forward_zero_terms = jnp.zeros((col_count,) + block_shape, jnp.float32)
        owner_reduced = scatter_columns(
            block_terms(
                tiles_local[level_index - 1],
                sources_local[level_index - 1],
                column_slot(targets_local[level_index - 1]),
                filled_local[level_index - 1],
                forward_gathered,
                forward_zero_terms,
                False,
            ),
        )
        forward.append(
            apply_inverse(inverse_local[level_index], rhs_local[level_index] - owner_reduced)
        )
    backward = [apply_transposed(inverse_local[last_level], forward[-1])]
    for level_index in range(last_level - 1, -1, -1):
        gathered = gather_columns(backward[0])
        solved = forward[level_index]
        zero_terms = jnp.zeros((row_count,) + block_shape, jnp.float32)
        totals = block_terms(
            tiles_local[level_index],
            column_slot(targets_local[level_index]),
            sources_local[level_index],
            filled_local[level_index],
            gathered,
            zero_terms,
            True,
        )
        reduced = scatter_sum(totals, "row")
        backward.insert(0, apply_transposed(inverse_local[level_index], solved - reduced))
    return jnp.stack(forward), jnp.stack(backward)


def per_device(rhs, diag_inverse, update_blocks, source_slot, target_slot, block_count):
    rhs_local = rhs[:, 0, 0]
    shared = (diag_inverse[:, 0, 0], update_blocks[:, 0, 0], source_slot[:, 0, 0], target_slot[:, 0, 0],
              block_count[:, 0, 0])
    width = rhs_local.shape[-1]
    chunks = CHUNKS if width % (CHUNKS * 128) == 0 else 1
    step = width // chunks
    results = [solve_columns(rhs_local[..., k * step:(k + 1) * step], *shared) for k in range(chunks)]
    forward_out = jnp.concatenate([r[0] for r in results], axis=-1)[:, None, None]
    backward_out = jnp.concatenate([r[1] for r in results], axis=-1)[:, None, None]
    return (forward_out, backward_out)


def solution(mesh):
    rows, cols = mesh.devices.shape
    split = Mesh(mesh.devices.reshape(rows, cols // 2, 2), ("row", "chip", "core"))
    col = ("chip", "core")
    in_specs = (
        P(None, "row", col, None, None),
        P(None, "row", col, None, None),
        P(None, "row", col, None, None, None),
        P(None, "row", col, None),
        P(None, "row", col, None),
        P(None, "row", col),
    )
    out_specs = (P(None, "row", col, None, None), P(None, "row", col, None, None))
    return jax.shard_map(
        per_device, mesh=split, in_specs=in_specs, out_specs=out_specs, check_vma=False
    )
```

```python
import functools
import math

import jax
import jax.numpy as jnp
from jax import lax
from jax.experimental import pallas as pl
from jax.experimental.pallas import tpu as pltpu
from jax.sharding import Mesh
from jax.sharding import PartitionSpec as P

GROUP = 8


def apply_inverse(inverse, values):
    return jnp.einsum("...st,...tn->...sn", inverse, values, precision=lax.Precision.HIGHEST)


def apply_transposed(inverse, values):
    return jnp.einsum("...ts,...tn->...sn", inverse, values, precision=lax.Precision.HIGHEST)


def _split(values):
    high = values.astype(jnp.bfloat16)
    low = (values - high.astype(jnp.float32)).astype(jnp.bfloat16)
    return high, low


def _terms_kernel(transposed, group, picked_ref, placed_ref, filled_ref, tiles_ref, operand_ref, out_ref, split_ref):
    step = pl.program_id(0)

    @pl.when(step == 0)
    def _():
        out_ref[...] = jnp.zeros_like(out_ref)
        for source in range(operand_ref.shape[0]):
            high, low = _split(operand_ref[source])
            split_ref[source] = jnp.concatenate([high, low, high], axis=0)

    filled = filled_ref[0]
    for g in range(group):
        b = step * group + g

        @pl.when(b < filled)
        def _():
            high, low = _split(tiles_ref[g])
            values = split_ref[picked_ref[b]]
            if transposed:
                stacked = jnp.concatenate([high, high, low], axis=0)
                product = lax.dot_general(stacked, values, (((0,), (0,)), ((), ())),
                                          preferred_element_type=jnp.float32)
            else:
                stacked = jnp.concatenate([high, high, low], axis=1)
                product = jnp.dot(stacked, values, preferred_element_type=jnp.float32)
            out_ref[placed_ref[b]] += product


def block_terms_kernel(tile_stack, picked, placed, filled, operand, count, transposed):
    slot_count, s, _ = tile_stack.shape
    n_src, _, width = operand.shape
    group = math.gcd(slot_count, GROUP)
    steps = slot_count // group

    def tile_map(j, picked_ref, placed_ref, filled_ref):
        last = jnp.maximum(filled_ref[0] - 1, 0) // group
        return (jnp.minimum(j, last), 0, 0)

    grid_spec = pltpu.PrefetchScalarGridSpec(
        num_scalar_prefetch=3,
        grid=(steps,),
        in_specs=[
            pl.BlockSpec((group, s, s), tile_map),
            pl.BlockSpec((n_src, s, width), lambda j, *_: (0, 0, 0)),
        ],
        out_specs=pl.BlockSpec((count, s, width), lambda j, *_: (0, 0, 0)),
        scratch_shapes=[pltpu.VMEM((n_src, 3 * s, width), jnp.bfloat16)],
    )
    flops = 2 * slot_count * s * s * width
    return pl.pallas_call(
        functools.partial(_terms_kernel, transposed, group),
        grid_spec=grid_spec,
        out_shape=jax.ShapeDtypeStruct((count, s, width), jnp.float32),
        compiler_params=pltpu.CompilerParams(dimension_semantics=("arbitrary",)),
        cost_estimate=pl.CostEstimate(flops=flops, bytes_accessed=4 * (slot_count * s * s + 2 * n_src * s * width), transcendentals=0),
    )(jnp.clip(picked, 0, n_src - 1), jnp.clip(placed, 0, count - 1), jnp.reshape(filled, (1,)), tile_stack, operand)


def block_terms(tile_stack, picked, placed, filled, operand, totals, transposed):
    return block_terms_kernel(tile_stack, picked, placed, filled, operand, totals.shape[0], transposed)


def gather_blocks(block, axis, count):
    stacked = jnp.broadcast_to(block[None], (count,) + block.shape)
    return lax.all_to_all(stacked, axis, 0, 0, tiled=True)


def scatter_sum(parts, axis):
    return lax.all_to_all(parts, axis, 0, 0, tiled=True).sum(axis=0)


def column_slot(position):
    cores = lax.axis_size("core")
    core_rel = (position % cores - lax.axis_index("core")) % cores
    return core_rel * lax.axis_size("chip") + position // cores


def gather_columns(block):
    chips = lax.axis_size("chip")
    cores = lax.axis_size("core")
    by_chip = gather_blocks(block, "chip", chips)
    other = lax.ppermute(by_chip, "core", [(j, (j + 1) % cores) for j in range(cores)])
    return jnp.concatenate([by_chip, other], axis=0)


def scatter_columns(parts):
    chips = lax.axis_size("chip")
    cores = lax.axis_size("core")
    chip_sums = parts[:chips] + lax.ppermute(parts[chips:], "core", [(j, (j + 1) % cores) for j in range(cores)])
    return scatter_sum(chip_sums, "chip")


def per_device(rhs, diag_inverse, update_blocks, source_slot, target_slot, block_count):
    levels = rhs.shape[0]
    last_level = levels - 1
    rhs_local = rhs[:, 0, 0]
    inverse_local = diag_inverse[:, 0, 0]
    tiles_local = update_blocks[:, 0, 0]
    sources_local = source_slot[:, 0, 0]
    targets_local = target_slot[:, 0, 0]
    filled_local = block_count[:, 0, 0]
    row_count = lax.axis_size("row")
    col_count = lax.axis_size("chip") * lax.axis_size("core")
    block_shape = rhs_local.shape[1:]
    forward = [apply_inverse(inverse_local[0], rhs_local[0])]
    for level_index in range(1, levels):
        forward_gathered = gather_blocks(forward[-1], "row", row_count)
        forward_zero_terms = jnp.zeros((col_count,) + block_shape, jnp.float32)
        owner_reduced = scatter_columns(
            block_terms(
                tiles_local[level_index - 1],
                sources_local[level_index - 1],
                column_slot(targets_local[level_index - 1]),
                filled_local[level_index - 1],
                forward_gathered,
                forward_zero_terms,
                False,
            ),
        )
        forward.append(
            apply_inverse(inverse_local[level_index], rhs_local[level_index] - owner_reduced)
        )
    backward = [apply_transposed(inverse_local[last_level], forward[-1])]
    for level_index in range(last_level - 1, -1, -1):
        gathered = gather_columns(backward[0])
        solved = forward[level_index]
        zero_terms = jnp.zeros((row_count,) + block_shape, jnp.float32)
        totals = block_terms(
            tiles_local[level_index],
            column_slot(targets_local[level_index]),
            sources_local[level_index],
            filled_local[level_index],
            gathered,
            zero_terms,
            True,
        )
        reduced = scatter_sum(totals, "row")
        backward.insert(0, apply_transposed(inverse_local[level_index], solved - reduced))
    forward_out = jnp.stack(forward)[:, None, None]
    backward_out = jnp.stack(backward)[:, None, None]
    return (forward_out, backward_out)


def solution(mesh):
    rows, cols = mesh.devices.shape
    split = Mesh(mesh.devices.reshape(rows, cols // 2, 2), ("row", "chip", "core"))
    col = ("chip", "core")
    in_specs = (
        P(None, "row", col, None, None),
        P(None, "row", col, None, None),
        P(None, "row", col, None, None, None),
        P(None, "row", col, None),
        P(None, "row", col, None),
        P(None, "row", col),
    )
    out_specs = (P(None, "row", col, None, None), P(None, "row", col, None, None))
    return jax.shard_map(
        per_device, mesh=split, in_specs=in_specs, out_specs=out_specs, check_vma=False
    )
```

```python
import functools
import math

import jax
import jax.numpy as jnp
from jax import lax
from jax.experimental import pallas as pl
from jax.experimental.pallas import tpu as pltpu
from jax.sharding import Mesh
from jax.sharding import PartitionSpec as P

GROUP = 8


def apply_inverse(inverse, values):
    return jnp.einsum("...st,...tn->...sn", inverse, values, precision=lax.Precision.HIGHEST)


def apply_transposed(inverse, values):
    return jnp.einsum("...ts,...tn->...sn", inverse, values, precision=lax.Precision.HIGHEST)


def _split(values):
    high = values.astype(jnp.bfloat16)
    low = (values - high.astype(jnp.float32)).astype(jnp.bfloat16)
    return high, low


def _terms_kernel(transposed, pairs_per_step, tile_ref, first_ref, second_ref, source_ref, live_ref, *refs):
    tiles = refs[:2 * pairs_per_step]
    operand_ref, out_ref, split_ref = refs[2 * pairs_per_step:]
    step = pl.program_id(0)

    @pl.when(step == 0)
    def _():
        out_ref[...] = jnp.zeros_like(out_ref)
        for source in range(operand_ref.shape[0]):
            high, low = _split(operand_ref[source])
            split_ref[source] = jnp.concatenate([high, low, high], axis=0)

    for g in range(pairs_per_step):
        p = step * pairs_per_step + g

        @pl.when(live_ref[p] > 0)
        def _():
            tile = jnp.concatenate([tiles[2 * g][0], tiles[2 * g + 1][0]], axis=1 if transposed else 0)
            high, low = _split(tile)
            values = split_ref[source_ref[p]]
            if transposed:
                stacked = jnp.concatenate([high, high, low], axis=0)
                product = lax.dot_general(stacked, values, (((0,), (0,)), ((), ())),
                                          preferred_element_type=jnp.float32)
            else:
                stacked = jnp.concatenate([high, high, low], axis=1)
                product = jnp.dot(stacked, values, preferred_element_type=jnp.float32)
            rows = product.shape[0] // 2
            out_ref[first_ref[p]] += product[:rows]

            @pl.when(live_ref[p] > 1)
            def _():
                out_ref[second_ref[p]] += product[rows:]


def pair_blocks(picked, placed, filled, n_src):
    slot_count = picked.shape[0]
    span = slot_count + n_src
    span += span % 2
    index = jnp.arange(slot_count, dtype=jnp.int32)
    key = jnp.where(index < filled, jnp.clip(picked, 0, n_src - 1), n_src)
    order = jnp.argsort(key, stable=True).astype(jnp.int32)
    sorted_key = key[order]
    counts = jnp.zeros((n_src + 1,), jnp.int32).at[key].add(1)
    starts = jnp.cumsum(counts) - counts
    padded = (counts[:n_src] + 1) // 2 * 2
    padded_starts = jnp.cumsum(padded) - padded
    rank = index - starts[sorted_key]
    live = sorted_key < n_src
    position = jnp.where(live, padded_starts[jnp.minimum(sorted_key, n_src - 1)] + rank, span)
    slots = jnp.full((span + 1,), -1, jnp.int32).at[position].set(order)[:span].reshape(span // 2, 2)
    first, second = slots[:, 0], slots[:, 1]
    has_second = second >= 0
    second = jnp.where(has_second, second, jnp.maximum(first, 0))
    first = jnp.maximum(first, 0)
    live_count = jnp.where(slots[:, 0] >= 0, 1 + has_second.astype(jnp.int32), 0)
    return first, second, live_count


def block_terms_kernel(tile_stack, picked, placed, filled, operand, count, transposed):
    slot_count, s, _ = tile_stack.shape
    n_src, _, width = operand.shape
    first, second, live = pair_blocks(picked, placed, filled, n_src)
    pair_count = first.shape[0]
    pairs_per_step = 4
    steps = -(-pair_count // pairs_per_step)
    extra = steps * pairs_per_step - pair_count
    first = jnp.pad(first, (0, extra))
    second = jnp.pad(second, (0, extra))
    live = jnp.pad(live, (0, extra))
    source = jnp.clip(picked, 0, n_src - 1)[first]
    target_first = jnp.clip(placed, 0, count - 1)[first]
    target_second = jnp.clip(placed, 0, count - 1)[second]
    tile_index = jnp.stack([first, second], axis=1).reshape(-1)

    def tile_map(k):
        return lambda j, tile_ref, *_: (tile_ref[j * 2 * pairs_per_step + k], 0, 0)

    grid_spec = pltpu.PrefetchScalarGridSpec(
        num_scalar_prefetch=5,
        grid=(steps,),
        in_specs=[pl.BlockSpec((1, s, s), tile_map(k)) for k in range(2 * pairs_per_step)]
        + [pl.BlockSpec((n_src, s, width), lambda j, *_: (0, 0, 0))],
        out_specs=pl.BlockSpec((count, s, width), lambda j, *_: (0, 0, 0)),
        scratch_shapes=[pltpu.VMEM((n_src, 3 * s, width), jnp.bfloat16)],
    )
    flops = 2 * slot_count * s * s * width
    return pl.pallas_call(
        functools.partial(_terms_kernel, transposed, pairs_per_step),
        grid_spec=grid_spec,
        out_shape=jax.ShapeDtypeStruct((count, s, width), jnp.float32),
        compiler_params=pltpu.CompilerParams(dimension_semantics=("arbitrary",)),
        cost_estimate=pl.CostEstimate(flops=flops, bytes_accessed=4 * (slot_count * s * s + 2 * n_src * s * width), transcendentals=0),
    )(tile_index, target_first, target_second, source, live, *([tile_stack] * (2 * pairs_per_step)), operand)


def block_terms(tile_stack, picked, placed, filled, operand, totals, transposed):
    return block_terms_kernel(tile_stack, picked, placed, filled, operand, totals.shape[0], transposed)


def gather_blocks(block, axis, count):
    stacked = jnp.broadcast_to(block[None], (count,) + block.shape)
    return lax.all_to_all(stacked, axis, 0, 0, tiled=True)


def scatter_sum(parts, axis):
    return lax.all_to_all(parts, axis, 0, 0, tiled=True).sum(axis=0)


def column_slot(position):
    cores = lax.axis_size("core")
    core_rel = (position % cores - lax.axis_index("core")) % cores
    return core_rel * lax.axis_size("chip") + position // cores


def gather_columns(block):
    chips = lax.axis_size("chip")
    cores = lax.axis_size("core")
    by_chip = gather_blocks(block, "chip", chips)
    other = lax.ppermute(by_chip, "core", [(j, (j + 1) % cores) for j in range(cores)])
    return jnp.concatenate([by_chip, other], axis=0)


def scatter_columns(parts):
    chips = lax.axis_size("chip")
    cores = lax.axis_size("core")
    chip_sums = parts[:chips] + lax.ppermute(parts[chips:], "core", [(j, (j + 1) % cores) for j in range(cores)])
    return scatter_sum(chip_sums, "chip")


def per_device(rhs, diag_inverse, update_blocks, source_slot, target_slot, block_count):
    levels = rhs.shape[0]
    last_level = levels - 1
    rhs_local = rhs[:, 0, 0]
    inverse_local = diag_inverse[:, 0, 0]
    tiles_local = update_blocks[:, 0, 0]
    sources_local = source_slot[:, 0, 0]
    targets_local = target_slot[:, 0, 0]
    filled_local = block_count[:, 0, 0]
    row_count = lax.axis_size("row")
    col_count = lax.axis_size("chip") * lax.axis_size("core")
    block_shape = rhs_local.shape[1:]
    forward = [apply_inverse(inverse_local[0], rhs_local[0])]
    for level_index in range(1, levels):
        forward_gathered = gather_blocks(forward[-1], "row", row_count)
        forward_zero_terms = jnp.zeros((col_count,) + block_shape, jnp.float32)
        owner_reduced = scatter_columns(
            block_terms(
                tiles_local[level_index - 1],
                sources_local[level_index - 1],
                column_slot(targets_local[level_index - 1]),
                filled_local[level_index - 1],
                forward_gathered,
                forward_zero_terms,
                False,
            ),
        )
        forward.append(
            apply_inverse(inverse_local[level_index], rhs_local[level_index] - owner_reduced)
        )
    backward = [apply_transposed(inverse_local[last_level], forward[-1])]
    for level_index in range(last_level - 1, -1, -1):
        gathered = gather_columns(backward[0])
        solved = forward[level_index]
        zero_terms = jnp.zeros((row_count,) + block_shape, jnp.float32)
        totals = block_terms(
            tiles_local[level_index],
            column_slot(targets_local[level_index]),
            sources_local[level_index],
            filled_local[level_index],
            gathered,
            zero_terms,
            True,
        )
        reduced = scatter_sum(totals, "row")
        backward.insert(0, apply_transposed(inverse_local[level_index], solved - reduced))
    forward_out = jnp.stack(forward)[:, None, None]
    backward_out = jnp.stack(backward)[:, None, None]
    return (forward_out, backward_out)


def solution(mesh):
    rows, cols = mesh.devices.shape
    split = Mesh(mesh.devices.reshape(rows, cols // 2, 2), ("row", "chip", "core"))
    col = ("chip", "core")
    in_specs = (
        P(None, "row", col, None, None),
        P(None, "row", col, None, None),
        P(None, "row", col, None, None, None),
        P(None, "row", col, None),
        P(None, "row", col, None),
        P(None, "row", col),
    )
    out_specs = (P(None, "row", col, None, None), P(None, "row", col, None, None))
    return jax.shard_map(
        per_device, mesh=split, in_specs=in_specs, out_specs=out_specs, check_vma=False
    )
```

```python
import functools
import math

import jax
import jax.numpy as jnp
from jax import lax
from jax.experimental import pallas as pl
from jax.experimental.pallas import tpu as pltpu
from jax.sharding import Mesh
from jax.sharding import PartitionSpec as P

GROUP = 8


def apply_inverse(inverse, values):
    return jnp.einsum("...st,...tn->...sn", inverse, values, precision=lax.Precision.HIGHEST)


def apply_transposed(inverse, values):
    return jnp.einsum("...ts,...tn->...sn", inverse, values, precision=lax.Precision.HIGHEST)


def _split(values):
    high = values.astype(jnp.bfloat16)
    low = (values - high.astype(jnp.float32)).astype(jnp.bfloat16)
    return high, low


def _terms_kernel(transposed, pairs_per_step, tile_ref, first_ref, second_ref, source_ref, live_ref, *refs):
    tiles = refs[:2 * pairs_per_step]
    operand_ref, out_ref, split_ref = refs[2 * pairs_per_step:]
    step = pl.program_id(0)

    @pl.when(step == 0)
    def _():
        out_ref[...] = jnp.zeros_like(out_ref)
        for source in range(operand_ref.shape[0]):
            high, low = _split(operand_ref[source])
            split_ref[source] = jnp.concatenate([high, low, high], axis=0)

    for g in range(pairs_per_step):
        p = step * pairs_per_step + g

        @pl.when(live_ref[p] > 0)
        def _():
            tile = jnp.concatenate([tiles[2 * g][0], tiles[2 * g + 1][0]], axis=1 if transposed else 0)
            high, low = _split(tile)
            values = split_ref[source_ref[p]]
            if transposed:
                stacked = jnp.concatenate([high, high, low], axis=0)
                product = lax.dot_general(stacked, values, (((0,), (0,)), ((), ())),
                                          preferred_element_type=jnp.float32)
            else:
                stacked = jnp.concatenate([high, high, low], axis=1)
                product = jnp.dot(stacked, values, preferred_element_type=jnp.float32)
            rows = product.shape[0] // 2
            out_ref[first_ref[p]] += product[:rows]

            @pl.when(live_ref[p] > 1)
            def _():
                out_ref[second_ref[p]] += product[rows:]


def pair_blocks(picked, filled, n_src):
    slot_count = picked.shape[0]
    span = slot_count + n_src
    span += span % 2
    index = jnp.arange(slot_count, dtype=jnp.int32)
    key = jnp.where(index < filled, jnp.clip(picked, 0, n_src - 1), n_src)
    order = jnp.argsort(key, stable=True).astype(jnp.int32)
    sorted_key = key[order]
    counts = jnp.zeros((n_src + 1,), jnp.int32).at[key].add(1)
    starts = jnp.cumsum(counts) - counts
    padded = (counts[:n_src] + 1) // 2 * 2
    padded_starts = jnp.cumsum(padded) - padded
    rank = index - starts[sorted_key]
    live = sorted_key < n_src
    position = jnp.where(live, padded_starts[jnp.minimum(sorted_key, n_src - 1)] + rank, span)
    slots = jnp.full((span + 1,), -1, jnp.int32).at[position].set(order)[:span].reshape(span // 2, 2)
    first, second = slots[:, 0], slots[:, 1]
    has_second = second >= 0
    second = jnp.where(has_second, second, jnp.maximum(first, 0))
    first = jnp.maximum(first, 0)
    live_count = jnp.where(slots[:, 0] >= 0, 1 + has_second.astype(jnp.int32), 0)
    return first, second, live_count


def block_terms_kernel(tile_stack, picked, placed, pairing, operand, count, transposed):
    slot_count, s, _ = tile_stack.shape
    n_src, _, width = operand.shape
    first, second, live = pairing
    pair_count = first.shape[0]
    pairs_per_step = 4
    steps = -(-pair_count // pairs_per_step)
    extra = steps * pairs_per_step - pair_count
    first = jnp.pad(first, (0, extra))
    second = jnp.pad(second, (0, extra))
    live = jnp.pad(live, (0, extra))
    source = jnp.clip(picked, 0, n_src - 1)[first]
    target_first = jnp.clip(placed, 0, count - 1)[first]
    target_second = jnp.clip(placed, 0, count - 1)[second]
    tile_index = jnp.stack([first, second], axis=1).reshape(-1)

    def tile_map(k):
        return lambda j, tile_ref, *_: (tile_ref[j * 2 * pairs_per_step + k], 0, 0)

    grid_spec = pltpu.PrefetchScalarGridSpec(
        num_scalar_prefetch=5,
        grid=(steps,),
        in_specs=[pl.BlockSpec((1, s, s), tile_map(k)) for k in range(2 * pairs_per_step)]
        + [pl.BlockSpec((n_src, s, width), lambda j, *_: (0, 0, 0))],
        out_specs=pl.BlockSpec((count, s, width), lambda j, *_: (0, 0, 0)),
        scratch_shapes=[pltpu.VMEM((n_src, 3 * s, width), jnp.bfloat16)],
    )
    flops = 2 * slot_count * s * s * width
    return pl.pallas_call(
        functools.partial(_terms_kernel, transposed, pairs_per_step),
        grid_spec=grid_spec,
        out_shape=jax.ShapeDtypeStruct((count, s, width), jnp.float32),
        compiler_params=pltpu.CompilerParams(dimension_semantics=("arbitrary",)),
        cost_estimate=pl.CostEstimate(flops=flops, bytes_accessed=4 * (slot_count * s * s + 2 * n_src * s * width), transcendentals=0),
    )(tile_index, target_first, target_second, source, live, *([tile_stack] * (2 * pairs_per_step)), operand)


def block_terms(tile_stack, picked, placed, pairing, operand, totals, transposed):
    return block_terms_kernel(tile_stack, picked, placed, pairing, operand, totals.shape[0], transposed)


def gather_blocks(block, axis, count):
    stacked = jnp.broadcast_to(block[None], (count,) + block.shape)
    return lax.all_to_all(stacked, axis, 0, 0, tiled=True)


def scatter_sum(parts, axis):
    return lax.all_to_all(parts, axis, 0, 0, tiled=True).sum(axis=0)


def column_slot(position):
    cores = lax.axis_size("core")
    core_rel = (position % cores - lax.axis_index("core")) % cores
    return core_rel * lax.axis_size("chip") + position // cores


def gather_columns(block):
    chips = lax.axis_size("chip")
    cores = lax.axis_size("core")
    by_chip = gather_blocks(block, "chip", chips)
    other = lax.ppermute(by_chip, "core", [(j, (j + 1) % cores) for j in range(cores)])
    return jnp.concatenate([by_chip, other], axis=0)


def scatter_columns(parts):
    chips = lax.axis_size("chip")
    cores = lax.axis_size("core")
    chip_sums = parts[:chips] + lax.ppermute(parts[chips:], "core", [(j, (j + 1) % cores) for j in range(cores)])
    return scatter_sum(chip_sums, "chip")


def per_device(rhs, diag_inverse, update_blocks, source_slot, target_slot, block_count):
    levels = rhs.shape[0]
    last_level = levels - 1
    rhs_local = rhs[:, 0, 0]
    inverse_local = diag_inverse[:, 0, 0]
    tiles_local = update_blocks[:, 0, 0]
    sources_local = source_slot[:, 0, 0]
    targets_local = target_slot[:, 0, 0]
    filled_local = block_count[:, 0, 0]
    row_count = lax.axis_size("row")
    col_count = lax.axis_size("chip") * lax.axis_size("core")
    block_shape = rhs_local.shape[1:]
    forward_pairs = jax.vmap(functools.partial(pair_blocks, n_src=row_count))(sources_local, filled_local)
    backward_picked = column_slot(targets_local)
    backward_pairs = jax.vmap(functools.partial(pair_blocks, n_src=col_count))(backward_picked, filled_local)
    forward = [apply_inverse(inverse_local[0], rhs_local[0])]
    for level_index in range(1, levels):
        forward_gathered = gather_blocks(forward[-1], "row", row_count)
        forward_zero_terms = jnp.zeros((col_count,) + block_shape, jnp.float32)
        owner_reduced = scatter_columns(
            block_terms(
                tiles_local[level_index - 1],
                sources_local[level_index - 1],
                column_slot(targets_local[level_index - 1]),
                tuple(t[level_index - 1] for t in forward_pairs),
                forward_gathered,
                forward_zero_terms,
                False,
            ),
        )
        forward.append(
            apply_inverse(inverse_local[level_index], rhs_local[level_index] - owner_reduced)
        )
    backward = [apply_transposed(inverse_local[last_level], forward[-1])]
    for level_index in range(last_level - 1, -1, -1):
        gathered = gather_columns(backward[0])
        solved = forward[level_index]
        zero_terms = jnp.zeros((row_count,) + block_shape, jnp.float32)
        totals = block_terms(
            tiles_local[level_index],
            backward_picked[level_index],
            sources_local[level_index],
            tuple(t[level_index] for t in backward_pairs),
            gathered,
            zero_terms,
            True,
        )
        reduced = scatter_sum(totals, "row")
        backward.insert(0, apply_transposed(inverse_local[level_index], solved - reduced))
    forward_out = jnp.stack(forward)[:, None, None]
    backward_out = jnp.stack(backward)[:, None, None]
    return (forward_out, backward_out)


def solution(mesh):
    rows, cols = mesh.devices.shape
    split = Mesh(mesh.devices.reshape(rows, cols // 2, 2), ("row", "chip", "core"))
    col = ("chip", "core")
    in_specs = (
        P(None, "row", col, None, None),
        P(None, "row", col, None, None),
        P(None, "row", col, None, None, None),
        P(None, "row", col, None),
        P(None, "row", col, None),
        P(None, "row", col),
    )
    out_specs = (P(None, "row", col, None, None), P(None, "row", col, None, None))
    return jax.shard_map(
        per_device, mesh=split, in_specs=in_specs, out_specs=out_specs, check_vma=False
    )
```

```python
import functools
import math

import jax
import jax.numpy as jnp
from jax import lax
from jax.experimental import pallas as pl
from jax.experimental.pallas import tpu as pltpu
from jax.sharding import Mesh
from jax.sharding import PartitionSpec as P

GROUP = 8


def apply_inverse(inverse, values):
    return jnp.einsum("...st,...tn->...sn", inverse, values, precision=lax.Precision.HIGHEST)


def apply_transposed(inverse, values):
    return jnp.einsum("...ts,...tn->...sn", inverse, values, precision=lax.Precision.HIGHEST)


def _split(values):
    high = values.astype(jnp.bfloat16)
    low = (values - high.astype(jnp.float32)).astype(jnp.bfloat16)
    return high, low


def _terms_kernel(transposed, pairs_per_step, tile_ref, first_ref, second_ref, source_ref, live_ref, *refs):
    tiles = refs[:2 * pairs_per_step]
    operand_ref, out_ref, split_ref = refs[2 * pairs_per_step:]
    step = pl.program_id(0)

    @pl.when(step == 0)
    def _():
        out_ref[...] = jnp.zeros_like(out_ref)
        for source in range(operand_ref.shape[0]):
            high, low = _split(operand_ref[source])
            split_ref[source] = jnp.concatenate([high, low, high], axis=0)

    for g in range(pairs_per_step):
        p = step * pairs_per_step + g

        @pl.when(live_ref[p] > 0)
        def _():
            tile = jnp.concatenate([tiles[2 * g][0], tiles[2 * g + 1][0]], axis=1 if transposed else 0)
            high, low = _split(tile)
            values = split_ref[source_ref[p]]
            if transposed:
                stacked = jnp.concatenate([high, high, low], axis=0)
                product = lax.dot_general(stacked, values, (((0,), (0,)), ((), ())),
                                          preferred_element_type=jnp.float32)
            else:
                stacked = jnp.concatenate([high, high, low], axis=1)
                product = jnp.dot(stacked, values, preferred_element_type=jnp.float32)
            rows = product.shape[0] // 2
            out_ref[first_ref[p]] += product[:rows]

            @pl.when(live_ref[p] > 1)
            def _():
                out_ref[second_ref[p]] += product[rows:]


def pair_blocks(picked, placed, filled, n_src, count):
    slot_count = picked.shape[0]
    span = slot_count + n_src
    span += span % 2
    index = jnp.arange(slot_count, dtype=jnp.int32)
    picked = jnp.clip(picked, 0, n_src - 1)
    placed = jnp.clip(placed, 0, count - 1)
    key = jnp.where(index < filled, picked, n_src)
    same = key[:, None] == key[None, :]
    rank = jnp.sum(same & (index[None, :] < index[:, None]), axis=1, dtype=jnp.int32)
    groups = jnp.arange(n_src, dtype=jnp.int32)
    member = key[:, None] == groups[None, :]
    counts = jnp.sum(member, axis=0, dtype=jnp.int32)
    padded = (counts + 1) // 2 * 2
    padded_starts = jnp.cumsum(padded) - padded
    start = jnp.sum(jnp.where(member, padded_starts[None, :], 0), axis=1, dtype=jnp.int32)
    position = jnp.where(key < n_src, start + rank, span)
    hit = position[None, :] == jnp.arange(span, dtype=jnp.int32)[:, None]
    used = jnp.any(hit, axis=1).reshape(span // 2, 2)

    def pick(values):
        return jnp.sum(jnp.where(hit, values[None, :], 0), axis=1, dtype=jnp.int32).reshape(span // 2, 2)

    tiles = pick(index)
    sources = pick(picked)
    targets = pick(placed)
    has_second = used[:, 1]
    second_tile = jnp.where(has_second, tiles[:, 1], tiles[:, 0])
    second_target = jnp.where(has_second, targets[:, 1], targets[:, 0])
    live = jnp.where(used[:, 0], 1 + has_second.astype(jnp.int32), 0)
    tile_index = jnp.stack([tiles[:, 0], second_tile], axis=1).reshape(-1)
    return tile_index, targets[:, 0], second_target, sources[:, 0], live


def block_terms_kernel(tile_stack, pairing, operand, count, transposed):
    slot_count, s, _ = tile_stack.shape
    n_src, _, width = operand.shape
    tile_index, target_first, target_second, source, live = pairing
    pair_count = live.shape[0]
    pairs_per_step = 4
    steps = -(-pair_count // pairs_per_step)
    extra = steps * pairs_per_step - pair_count
    tile_index = jnp.pad(tile_index, (0, 2 * extra))
    target_first = jnp.pad(target_first, (0, extra))
    target_second = jnp.pad(target_second, (0, extra))
    source = jnp.pad(source, (0, extra))
    live = jnp.pad(live, (0, extra))

    def tile_map(k):
        return lambda j, tile_ref, *_: (tile_ref[j * 2 * pairs_per_step + k], 0, 0)

    grid_spec = pltpu.PrefetchScalarGridSpec(
        num_scalar_prefetch=5,
        grid=(steps,),
        in_specs=[pl.BlockSpec((1, s, s), tile_map(k)) for k in range(2 * pairs_per_step)]
        + [pl.BlockSpec((n_src, s, width), lambda j, *_: (0, 0, 0))],
        out_specs=pl.BlockSpec((count, s, width), lambda j, *_: (0, 0, 0)),
        scratch_shapes=[pltpu.VMEM((n_src, 3 * s, width), jnp.bfloat16)],
    )
    flops = 2 * slot_count * s * s * width
    return pl.pallas_call(
        functools.partial(_terms_kernel, transposed, pairs_per_step),
        grid_spec=grid_spec,
        out_shape=jax.ShapeDtypeStruct((count, s, width), jnp.float32),
        compiler_params=pltpu.CompilerParams(dimension_semantics=("arbitrary",)),
        cost_estimate=pl.CostEstimate(flops=flops, bytes_accessed=4 * (slot_count * s * s + 2 * n_src * s * width), transcendentals=0),
    )(tile_index, target_first, target_second, source, live, *([tile_stack] * (2 * pairs_per_step)), operand)


def block_terms(tile_stack, picked, placed, pairing, operand, totals, transposed):
    return block_terms_kernel(tile_stack, pairing, operand, totals.shape[0], transposed)


def gather_blocks(block, axis, count):
    stacked = jnp.broadcast_to(block[None], (count,) + block.shape)
    return lax.all_to_all(stacked, axis, 0, 0, tiled=True)


def scatter_sum(parts, axis):
    return lax.all_to_all(parts, axis, 0, 0, tiled=True).sum(axis=0)


def column_slot(position):
    cores = lax.axis_size("core")
    core_rel = (position % cores - lax.axis_index("core")) % cores
    return core_rel * lax.axis_size("chip") + position // cores


def gather_columns(block):
    chips = lax.axis_size("chip")
    cores = lax.axis_size("core")
    by_chip = gather_blocks(block, "chip", chips)
    other = lax.ppermute(by_chip, "core", [(j, (j + 1) % cores) for j in range(cores)])
    return jnp.concatenate([by_chip, other], axis=0)


def scatter_columns(parts):
    chips = lax.axis_size("chip")
    cores = lax.axis_size("core")
    chip_sums = parts[:chips] + lax.ppermute(parts[chips:], "core", [(j, (j + 1) % cores) for j in range(cores)])
    return scatter_sum(chip_sums, "chip")


def per_device(rhs, diag_inverse, update_blocks, source_slot, target_slot, block_count):
    levels = rhs.shape[0]
    last_level = levels - 1
    rhs_local = rhs[:, 0, 0]
    inverse_local = diag_inverse[:, 0, 0]
    tiles_local = update_blocks[:, 0, 0]
    sources_local = source_slot[:, 0, 0]
    targets_local = target_slot[:, 0, 0]
    filled_local = block_count[:, 0, 0]
    row_count = lax.axis_size("row")
    col_count = lax.axis_size("chip") * lax.axis_size("core")
    block_shape = rhs_local.shape[1:]
    forward_pairs = jax.vmap(functools.partial(pair_blocks, n_src=row_count, count=col_count))(
        sources_local, column_slot(targets_local), filled_local)
    backward_picked = column_slot(targets_local)
    backward_pairs = jax.vmap(functools.partial(pair_blocks, n_src=col_count, count=row_count))(
        backward_picked, sources_local, filled_local)
    forward = [apply_inverse(inverse_local[0], rhs_local[0])]
    for level_index in range(1, levels):
        forward_gathered = gather_blocks(forward[-1], "row", row_count)
        forward_zero_terms = jnp.zeros((col_count,) + block_shape, jnp.float32)
        owner_reduced = scatter_columns(
            block_terms(
                tiles_local[level_index - 1],
                sources_local[level_index - 1],
                column_slot(targets_local[level_index - 1]),
                tuple(t[level_index - 1] for t in forward_pairs),
                forward_gathered,
                forward_zero_terms,
                False,
            ),
        )
        forward.append(
            apply_inverse(inverse_local[level_index], rhs_local[level_index] - owner_reduced)
        )
    backward = [apply_transposed(inverse_local[last_level], forward[-1])]
    for level_index in range(last_level - 1, -1, -1):
        gathered = gather_columns(backward[0])
        solved = forward[level_index]
        zero_terms = jnp.zeros((row_count,) + block_shape, jnp.float32)
        totals = block_terms(
            tiles_local[level_index],
            backward_picked[level_index],
            sources_local[level_index],
            tuple(t[level_index] for t in backward_pairs),
            gathered,
            zero_terms,
            True,
        )
        reduced = scatter_sum(totals, "row")
        backward.insert(0, apply_transposed(inverse_local[level_index], solved - reduced))
    forward_out = jnp.stack(forward)[:, None, None]
    backward_out = jnp.stack(backward)[:, None, None]
    return (forward_out, backward_out)


def solution(mesh):
    rows, cols = mesh.devices.shape
    split = Mesh(mesh.devices.reshape(rows, cols // 2, 2), ("row", "chip", "core"))
    col = ("chip", "core")
    in_specs = (
        P(None, "row", col, None, None),
        P(None, "row", col, None, None),
        P(None, "row", col, None, None, None),
        P(None, "row", col, None),
        P(None, "row", col, None),
        P(None, "row", col),
    )
    out_specs = (P(None, "row", col, None, None), P(None, "row", col, None, None))
    return jax.shard_map(
        per_device, mesh=split, in_specs=in_specs, out_specs=out_specs, check_vma=False
    )
```

```python
import functools
import math

import jax
import jax.numpy as jnp
from jax import lax
from jax.experimental import pallas as pl
from jax.experimental.pallas import tpu as pltpu
from jax.sharding import Mesh
from jax.sharding import PartitionSpec as P

GROUP = 8


def apply_inverse(inverse, values):
    return jnp.einsum("...st,...tn->...sn", inverse, values, precision=lax.Precision.HIGH)


def apply_transposed(inverse, values):
    return jnp.einsum("...ts,...tn->...sn", inverse, values, precision=lax.Precision.HIGH)


def _split(values):
    high = values.astype(jnp.bfloat16)
    low = (values - high.astype(jnp.float32)).astype(jnp.bfloat16)
    return high, low


def _terms_kernel(transposed, group, picked_ref, placed_ref, filled_ref, tiles_ref, operand_ref, out_ref, split_ref):
    step = pl.program_id(0)

    @pl.when(step == 0)
    def _():
        out_ref[...] = jnp.zeros_like(out_ref)
        for source in range(operand_ref.shape[0]):
            high, low = _split(operand_ref[source])
            split_ref[source] = jnp.concatenate([high, low, high], axis=0)

    filled = filled_ref[0]
    for g in range(group):
        b = step * group + g

        @pl.when(b < filled)
        def _():
            high, low = _split(tiles_ref[g])
            values = split_ref[picked_ref[b]]
            if transposed:
                stacked = jnp.concatenate([high, high, low], axis=0)
                product = lax.dot_general(stacked, values, (((0,), (0,)), ((), ())),
                                          preferred_element_type=jnp.float32)
            else:
                stacked = jnp.concatenate([high, high, low], axis=1)
                product = jnp.dot(stacked, values, preferred_element_type=jnp.float32)
            out_ref[placed_ref[b]] += product


def block_terms_kernel(tile_stack, picked, placed, filled, operand, count, transposed):
    slot_count, s, _ = tile_stack.shape
    n_src, _, width = operand.shape
    group = math.gcd(slot_count, GROUP)
    steps = slot_count // group

    def tile_map(j, picked_ref, placed_ref, filled_ref):
        last = jnp.maximum(filled_ref[0] - 1, 0) // group
        return (jnp.minimum(j, last), 0, 0)

    grid_spec = pltpu.PrefetchScalarGridSpec(
        num_scalar_prefetch=3,
        grid=(steps,),
        in_specs=[
            pl.BlockSpec((group, s, s), tile_map),
            pl.BlockSpec((n_src, s, width), lambda j, *_: (0, 0, 0)),
        ],
        out_specs=pl.BlockSpec((count, s, width), lambda j, *_: (0, 0, 0)),
        scratch_shapes=[pltpu.VMEM((n_src, 3 * s, width), jnp.bfloat16)],
    )
    flops = 2 * slot_count * s * s * width
    return pl.pallas_call(
        functools.partial(_terms_kernel, transposed, group),
        grid_spec=grid_spec,
        out_shape=jax.ShapeDtypeStruct((count, s, width), jnp.float32),
        compiler_params=pltpu.CompilerParams(dimension_semantics=("arbitrary",)),
        cost_estimate=pl.CostEstimate(flops=flops, bytes_accessed=4 * (slot_count * s * s + 2 * n_src * s * width), transcendentals=0),
    )(jnp.clip(picked, 0, n_src - 1), jnp.clip(placed, 0, count - 1), jnp.reshape(filled, (1,)), tile_stack, operand)


def block_terms(tile_stack, picked, placed, filled, operand, totals, transposed):
    return block_terms_kernel(tile_stack, picked, placed, filled, operand, totals.shape[0], transposed)


def gather_blocks(block, axis, count):
    stacked = jnp.broadcast_to(block[None], (count,) + block.shape)
    return lax.all_to_all(stacked, axis, 0, 0, tiled=True)


def scatter_sum(parts, axis):
    return lax.all_to_all(parts, axis, 0, 0, tiled=True).sum(axis=0)


def column_slot(position):
    cores = lax.axis_size("core")
    core_rel = (position % cores - lax.axis_index("core")) % cores
    return core_rel * lax.axis_size("chip") + position // cores


def gather_columns(block):
    chips = lax.axis_size("chip")
    cores = lax.axis_size("core")
    by_chip = gather_blocks(block, "chip", chips)
    other = lax.ppermute(by_chip, "core", [(j, (j + 1) % cores) for j in range(cores)])
    return jnp.concatenate([by_chip, other], axis=0)


def scatter_columns(parts):
    chips = lax.axis_size("chip")
    cores = lax.axis_size("core")
    chip_sums = parts[:chips] + lax.ppermute(parts[chips:], "core", [(j, (j + 1) % cores) for j in range(cores)])
    return scatter_sum(chip_sums, "chip")


def per_device(rhs, diag_inverse, update_blocks, source_slot, target_slot, block_count):
    levels = rhs.shape[0]
    last_level = levels - 1
    rhs_local = rhs[:, 0, 0]
    inverse_local = diag_inverse[:, 0, 0]
    tiles_local = update_blocks[:, 0, 0]
    sources_local = source_slot[:, 0, 0]
    targets_local = target_slot[:, 0, 0]
    filled_local = block_count[:, 0, 0]
    row_count = lax.axis_size("row")
    col_count = lax.axis_size("chip") * lax.axis_size("core")
    block_shape = rhs_local.shape[1:]
    forward = [apply_inverse(inverse_local[0], rhs_local[0])]
    for level_index in range(1, levels):
        forward_gathered = gather_blocks(forward[-1], "row", row_count)
        forward_zero_terms = jnp.zeros((col_count,) + block_shape, jnp.float32)
        owner_reduced = scatter_columns(
            block_terms(
                tiles_local[level_index - 1],
                sources_local[level_index - 1],
                column_slot(targets_local[level_index - 1]),
                filled_local[level_index - 1],
                forward_gathered,
                forward_zero_terms,
                False,
            ),
        )
        forward.append(
            apply_inverse(inverse_local[level_index], rhs_local[level_index] - owner_reduced)
        )
    backward = [apply_transposed(inverse_local[last_level], forward[-1])]
    for level_index in range(last_level - 1, -1, -1):
        gathered = gather_columns(backward[0])
        solved = forward[level_index]
        zero_terms = jnp.zeros((row_count,) + block_shape, jnp.float32)
        totals = block_terms(
            tiles_local[level_index],
            column_slot(targets_local[level_index]),
            sources_local[level_index],
            filled_local[level_index],
            gathered,
            zero_terms,
            True,
        )
        reduced = scatter_sum(totals, "row")
        backward.insert(0, apply_transposed(inverse_local[level_index], solved - reduced))
    forward_out = jnp.stack(forward)[:, None, None]
    backward_out = jnp.stack(backward)[:, None, None]
    return (forward_out, backward_out)


def solution(mesh):
    rows, cols = mesh.devices.shape
    split = Mesh(mesh.devices.reshape(rows, cols // 2, 2), ("row", "chip", "core"))
    col = ("chip", "core")
    in_specs = (
        P(None, "row", col, None, None),
        P(None, "row", col, None, None),
        P(None, "row", col, None, None, None),
        P(None, "row", col, None),
        P(None, "row", col, None),
        P(None, "row", col),
    )
    out_specs = (P(None, "row", col, None, None), P(None, "row", col, None, None))
    return jax.shard_map(
        per_device, mesh=split, in_specs=in_specs, out_specs=out_specs, check_vma=False
    )
```
